128 devices in a mesh: group: 8 (over y, core), member: 16 (over x, z).
Axes of the slice: x: 4, y: 4, z: 4, core: 2. Of those that a mesh axis runs over, the one named last changes fastest.
Arguments:
- queries: bfloat16 [2048, 64, 576], P(('group', 'member')), may hold values from -240 to 240
- latent_cache: bfloat16 [2048, 128, 576], P(('group', 'member')), may hold values from -4 to 4
- new_key: bfloat16 [2048, 576], P(('group', 'member')), may hold values from -4 to 4
- parent_beam: int32 [2048], P(('group', 'member')), may hold values from 0 to 3
- value_up: bfloat16 [64, 512, 128], P('member'), may hold values from -0.25 to 0.25
- out_proj: bfloat16 [8192, 3584], P('member', 'group'), may hold values from -0.0625 to 0.0625
- residual: bfloat16 [2048, 3584], P('member', 'group'), may hold values from -6 to 6
- expert_ids: int32 [2048, 8], P('member'), may hold values from 0 to 127, all different within a row; in each aligned block of 128 rows (0 to 127, 128 to 255, ...) at most 16 rows name the same one
- route_gates: float32 [2048, 8], P('member'), may hold values from 0.1 to 0.6
- w_gate: bfloat16 [128, 3584, 1024], P(('group', 'member')), may hold values from -0.09375 to 0.09375
- w_up: bfloat16 [128, 3584, 1024], P(('group', 'member')), may hold values from -0.09375 to 0.09375
- w_down: bfloat16 [128, 1024, 3584], P(('group', 'member')), may hold values from -0.1875 to 0.1875
Outputs:
- layer_out: bfloat16 [2048, 3584], P('member', 'group')
The draws below stay inside these ranges and needn't reach their ends.
Inputs may be any that keep to these rules, and one draw needn't show every extreme that they name: `expert_ids`: each row names 8 different experts. Within each aligned block of 128 rows no expert is named by more than 16 rows, a bound that some block reaches.
All inputs are finite; a program needn't handle non-finite values.
Results may differ from the reference program's by a relative error of at most 0.019.
Values may be sent and summed in bfloat16 or wider, within the bound.
No kernel may reach another device: no remote copies, remote signals or barrier semaphores. Data moves between devices by JAX's collectives and lax.ppermute only.
A program may use at most 128 MiB of HBM per device.

```python
import math
import jax
import jax.numpy as jnp
import numpy as np
from jax import lax

D = 3584
FF = 1024
HEADS = 64
LATENT = 512
ROPE = 64
VHEAD = 128
TOP = 8
BEAM = 4
CTX = 128
ROWS = 2048
EXPERTS = 128
BLOCK = 128
CAP = 16
N_MEMBER = 16


def draw_queries(key, part):
    first = jax.random.fold_in(key, 11)
    result = jax.random.truncated_normal(first, -4.0, 4.0, (ROWS, HEADS, LATENT + ROPE), jnp.float32)
    return result.astype(jnp.bfloat16)


def draw_latent_cache(key, part):
    first = jax.random.fold_in(key, 21)
    result = jax.random.truncated_normal(first, -4.0, 4.0, (ROWS, CTX, LATENT + ROPE), jnp.float32)
    return result.astype(jnp.bfloat16)


def place_ends(entries, own_key, low, high):
    extent = entries.shape
    index_at = [jax.random.randint(jax.random.fold_in(own_key, axis), (), 0, extent[axis]) for axis in range(len(extent))]
    entries = entries.at[tuple(index_at)].set(low)
    longest = extent.index(max(extent))
    index_at[longest] = (index_at[longest] + 1) % extent[longest]
    return entries.at[tuple(index_at)].set(high)


def steps_of(rng, extent, pieces, least, top_value):
    factor_of = 1.0
    for dim, parts in pieces:
        steps = jax.random.uniform(jax.random.fold_in(jax.random.fold_in(rng, 6), dim), (parts,), jnp.float32, least / len(pieces), top_value / len(pieces))
        factor_of = factor_of * jnp.repeat(jnp.exp(steps), extent[dim] // parts).reshape((-1,) + (1,) * (len(extent) - 1 - dim))
    return factor_of


def routed_block(stream_key, own, number, rows, count, top, most, slope):
    sequence = jax.random.permutation(stream_key, count)
    heavy_load, usual = load_shares(count, rows * top, most, slope, True), load_shares(count, rows * top, most, slope, False)
    places = jnp.arange(count)

    def named(sizes, rotation):
        used = int((sizes > 0).sum())
        fixed = max(1, used // 4)
        moved = fixed + (places - fixed + rotation * (used - fixed)) % max(1, count - fixed)
        return jnp.zeros((count,), jnp.int32).at[sequence[jnp.where(places < fixed, places, moved)]].set(jnp.asarray(sizes, jnp.int32))

    sizes = jnp.where(number % 4 == 0, named(heavy_load, number // 4), named(usual, number - number // 4 - 1))
    mixed = jax.random.permutation(jax.random.fold_in(own, 3), count)
    source_of, receiver = mixed[0:count // 2 * 2:2], mixed[1:count // 2 * 2:2]
    margin = jnp.minimum(sizes[source_of] - 1, most - sizes[receiver]) // 2
    margin = jnp.where((source_of == sequence[0]) | (receiver == sequence[0]) | (sizes[receiver] == 0), 0, jnp.maximum(margin, 0))
    moved = jax.random.randint(jax.random.fold_in(own, 4), (count // 2,), 0, 1 << 20) % (margin + 1)
    sizes = sizes.at[source_of].add(-moved).at[receiver].add(moved)
    items = jnp.searchsorted(jnp.cumsum(sizes), jnp.arange(rows * top), side="right").astype(jnp.int32)
    table = items.reshape(top, rows).T
    table = table[jax.random.permutation(jax.random.fold_in(own, 1), rows)]
    rotation = jax.random.randint(jax.random.fold_in(own, 2), (rows, 1), 0, top)
    return jnp.take_along_axis(table, (jnp.arange(top)[None, :] + rotation) % top, axis=1)


def load_shares(amount, total, most, slope, full):
    portions = [(1 << 20) // math.isqrt(standing ** slope) + 1 for standing in range(1, amount + 1)]
    largest = most if full else min(most, max(-(-total // amount), total * portions[0] // sum(portions)))
    least = 1 if total - largest >= amount - 1 else 0
    holding, rest = [largest] + [least] * (amount - 1), total - largest - least * (amount - 1)
    while rest > 0:
        candidates = [i for i in range(1, amount) if holding[i] < largest] or [i for i in range(1, amount) if holding[i] < most]
        whole, left = sum([portions[i] for i in candidates]), rest
        for i in candidates:
            more = min(most - holding[i], max(1, left * portions[i] // whole), rest)
            holding[i] = holding[i] + more
            rest = rest - more
    return np.array(holding)


def centred(own_key, shape, width, limit, split=(), kind=jnp.bfloat16):
    drawn = jax.random.normal(own_key, shape, jnp.float32) * width
    if len(split) > 0:
        drawn = steps_of(own_key, shape, split, -0.22, 0.18) * drawn
    return jnp.clip(drawn, min=-limit, max=limit).astype(kind)


def setup_inputs(seed: int = 0) -> dict:
    key_of = jax.random.split(jax.random.key(seed), 13)
    queries = draw_queries(jax.random.fold_in(key_of[12], 71), 0)
    latent_cache = draw_latent_cache(jax.random.fold_in(key_of[12], 71), 0)
    new_key = centred(key_of[2], (ROWS, LATENT + ROPE), 1.0, 4.0, ((0, 128),))
    parent_beam = place_ends(jax.random.randint(key_of[3], (ROWS,), 0, BEAM), jax.random.fold_in(key_of[3], 1), 0, BEAM - 1).astype(jnp.int32)
    value_up = centred(key_of[4], (HEADS, LATENT, VHEAD), LATENT ** -0.5, 0.25, ((0, 16),))
    out_proj = centred(key_of[5], (HEADS * VHEAD, D), (HEADS * VHEAD) ** -0.5, 0.0625, ((0, 16), (1, 8)))
    residual = centred(key_of[6], (ROWS, D), 1.0, 6.0, ((0, 16), (1, 8)))
    expert_ids_keys = jax.random.split(jax.random.fold_in(key_of[7], 1), ROWS // BLOCK)
    expert_ids_turns = jax.random.permutation(jax.random.fold_in(key_of[7], 3), ROWS // BLOCK)
    expert_ids = jax.vmap(lambda own, number: routed_block(jax.random.fold_in(key_of[7], 2), own, number, BLOCK, EXPERTS, TOP, CAP, 2))(expert_ids_keys, expert_ids_turns).reshape((ROWS, TOP))
    route_gates = jnp.clip(0.1 + 0.5 * jax.random.uniform(key_of[8], (ROWS, TOP), jnp.float32) ** steps_of(key_of[8], (ROWS, TOP), ((0, 16),), -0.2, 0.2), 0.1, 0.6)
    w_gate = centred(key_of[9], (EXPERTS, D, FF), D ** -0.5, 0.09375, ((0, 128),))
    w_up = centred(key_of[10], (EXPERTS, D, FF), D ** -0.5, 0.09375, ((0, 128),))
    w_down = centred(key_of[11], (EXPERTS, FF, D), FF ** -0.5, 0.1875, ((0, 128),))
    return dict(queries=queries, latent_cache=latent_cache, new_key=new_key, parent_beam=parent_beam, value_up=value_up, out_proj=out_proj, residual=residual, expert_ids=expert_ids, route_gates=route_gates, w_gate=w_gate, w_up=w_up, w_down=w_down)


def attend_block(block):
    asked, keys = block
    scale = (VHEAD + ROPE) ** -0.5
    scores = jnp.einsum("rhw,rcw->rhc", asked.astype(jnp.float32), keys.astype(jnp.float32)) * scale
    shifted = jnp.exp(scores - jnp.max(scores, axis=-1, keepdims=True))
    weights = (shifted / jnp.sum(shifted, axis=-1, keepdims=True)).astype(jnp.bfloat16)
    weights = lax.optimization_barrier(weights)
    values = keys[:, :, :LATENT].astype(jnp.float32)
    mixed = jnp.einsum("rhc,rcl->rhl", weights.astype(jnp.float32), values)
    return mixed.astype(jnp.bfloat16)


def reference(queries, latent_cache, new_key, parent_beam, value_up, out_proj, residual, expert_ids, route_gates, w_gate, w_up, w_down):
    row_index = jnp.arange(ROWS, dtype=jnp.int32)
    parent = ((row_index // BEAM) * BEAM + parent_beam).astype(jnp.int32)
    keys = jnp.concatenate([jnp.take(latent_cache, parent, axis=0), new_key[:, None, :]], axis=1)
    blocks = ROWS // 128
    latent_out = lax.map(attend_block, (queries.reshape(blocks, 128, HEADS, LATENT + ROPE), keys.reshape(blocks, 128, CTX + 1, LATENT + ROPE)))
    latent_out = lax.optimization_barrier(latent_out.reshape(ROWS, HEADS, LATENT))
    per_head = jnp.einsum("rhl,hlv->rhv", latent_out.astype(jnp.float32), value_up.astype(jnp.float32)).astype(jnp.bfloat16)
    per_head = per_head.reshape(ROWS, HEADS * VHEAD)
    span = (HEADS // N_MEMBER) * VHEAD
    attention = jnp.zeros((ROWS, D), jnp.float32)
    for member in range(N_MEMBER):
        partial_sum = jnp.dot(per_head[:, member * span:(member + 1) * span], out_proj[member * span:(member + 1) * span], preferred_element_type=jnp.float32)
        rounded = lax.optimization_barrier(partial_sum.astype(jnp.bfloat16))
        attention = attention + rounded.astype(jnp.float32)
    hidden_in = (residual.astype(jnp.float32) + attention).astype(jnp.bfloat16)
    most_rows = N_MEMBER * CAP

    def expert_step(total, item):
        index, gate_weights, up_weights, down_weights = item
        named = expert_ids == index
        weight = jnp.sum(jnp.where(named, route_gates, jnp.zeros_like(route_gates)), axis=1)
        chosen = jnp.any(named, axis=1)
        picked = jnp.nonzero(chosen, size=most_rows, fill_value=0)[0]
        live = jnp.arange(most_rows) < jnp.sum(chosen.astype(jnp.int32))
        rows_in = hidden_in[picked]
        gate = jnp.dot(rows_in, gate_weights, preferred_element_type=jnp.float32)
        upper = jnp.dot(rows_in, up_weights, preferred_element_type=jnp.float32)
        inner = (jax.nn.silu(gate) * upper).astype(jnp.bfloat16)
        output = lax.optimization_barrier(jnp.dot(inner, down_weights, preferred_element_type=jnp.float32).astype(jnp.bfloat16))
        term = weight[picked][:, None] * output.astype(jnp.float32)
        term = jnp.where(live[:, None], term, jnp.zeros_like(term))
        return total.at[picked].add(term), None

    total, unused = lax.scan(expert_step, jnp.zeros((ROWS, D), jnp.float32), (jnp.arange(EXPERTS, dtype=jnp.int32), w_gate, w_up, w_down))
    return (hidden_in.astype(jnp.float32) + total).astype(jnp.bfloat16)
```

```python
import jax
import jax.numpy as jnp
from jax import lax
from jax.sharding import PartitionSpec as P

ROPE = 64
VHEAD = 128
TOP = 8
BEAM = 4


def per_device(
    queries,
    latent_cache,
    new_key,
    parent_beam,
    value_up,
    out_proj,
    residual,
    expert_ids,
    route_gates,
    w_gate,
    w_up,
    w_down,
):
    rows = queries.shape[0]
    latent = value_up.shape[1]
    members = lax.axis_size("member")
    groups = lax.axis_size("group")
    experts = groups * members
    columns = out_proj.shape[1]
    scale = (VHEAD + ROPE) ** (-0.5)
    local_rows = jnp.arange(rows, dtype=jnp.int32)
    parent = local_rows // BEAM * BEAM + parent_beam
    keys = jnp.concatenate([jnp.take(latent_cache, parent, axis=0), new_key[:, None, :]], axis=1)
    scores = jnp.einsum("rhw,rcw->rhc", queries, keys, preferred_element_type=jnp.float32) * scale
    shifted = jnp.exp(scores - jnp.max(scores, axis=-1, keepdims=True))
    weights = (shifted / jnp.sum(shifted, axis=-1, keepdims=True)).astype(jnp.bfloat16)
    latent_out = jnp.einsum(
        "rhc,rcl->rhl", weights, keys[:, :, :latent], preferred_element_type=jnp.float32
    ).astype(jnp.bfloat16)
    by_heads = lax.all_to_all(latent_out, "member", split_axis=1, concat_axis=0, tiled=True)
    per_head = jnp.einsum(
        "rhl,hlv->rhv", by_heads, value_up, preferred_element_type=jnp.float32
    ).astype(jnp.bfloat16)
    per_head = per_head.reshape(per_head.shape[0], per_head.shape[1] * per_head.shape[2])
    partial_sums = jnp.dot(
        lax.all_gather(per_head, "group", axis=0, tiled=True),
        out_proj,
        preferred_element_type=jnp.float32,
    )
    pieces = lax.all_to_all(
        partial_sums.astype(jnp.bfloat16).reshape(members, -1, columns),
        "member",
        split_axis=0,
        concat_axis=0,
        tiled=True,
    )
    attention = jnp.sum(pieces.astype(jnp.float32), axis=0)
    hidden_in = (residual.astype(jnp.float32) + attention).astype(jnp.bfloat16)
    block_rows = hidden_in.shape[0]
    capacity = max(2, 2 * rows * TOP // members)
    flat_ids = expert_ids.reshape(-1)
    onehot = (flat_ids[:, None] == jnp.arange(experts, dtype=jnp.int32)[None, :]).astype(jnp.int32)
    ranking = jnp.sum((jnp.cumsum(onehot, axis=0) - onehot) * onehot, axis=1)
    slot_index = flat_ids * capacity + ranking
    positions = jnp.arange(experts * capacity, dtype=jnp.int32)
    matches = (positions[:, None] == slot_index[None, :]).reshape(
        experts * capacity, block_rows, TOP
    )
    send_map = jnp.any(matches, axis=2).astype(jnp.bfloat16)
    outgoing = jnp.dot(send_map, hidden_in, preferred_element_type=jnp.float32).astype(jnp.bfloat16)
    arrived = lax.all_to_all(
        outgoing.reshape(experts, capacity, columns),
        ("group", "member"),
        split_axis=0,
        concat_axis=0,
        tiled=True,
    )
    expert_rows = (
        arrived.reshape(groups, members, capacity, columns)
        .transpose(1, 2, 0, 3)
        .reshape(members * capacity, groups * columns)
    )
    gate = jnp.dot(expert_rows, w_gate[0], preferred_element_type=jnp.float32)
    upper = jnp.dot(expert_rows, w_up[0], preferred_element_type=jnp.float32)
    inner = (jax.nn.silu(gate) * upper).astype(jnp.bfloat16)
    results = jnp.dot(inner, w_down[0], preferred_element_type=jnp.float32).astype(jnp.bfloat16)
    arranged = (
        results.reshape(members, capacity, groups, columns)
        .transpose(2, 0, 1, 3)
        .reshape(experts, capacity, columns)
    )
    returned = lax.all_to_all(
        arranged, ("group", "member"), split_axis=0, concat_axis=0, tiled=True
    )
    returned = returned.reshape(experts * capacity, columns)
    picked = returned[slot_index.reshape(block_rows, TOP)].astype(jnp.float32)
    mixed = jnp.sum(route_gates[:, :, None] * picked, axis=1)
    return (hidden_in.astype(jnp.float32) + mixed).astype(jnp.bfloat16)


def solution(mesh):
    in_specs = (
        P(("group", "member"), None, None),
        P(("group", "member"), None, None),
        P(("group", "member"), None),
        P(("group", "member")),
        P("member", None, None),
        P("member", "group"),
        P("member", "group"),
        P("member", None),
        P("member", None),
        P(("group", "member"), None, None),
        P(("group", "member"), None, None),
        P(("group", "member"), None, None),
    )
    out_specs = P("member", "group")
    return jax.shard_map(
        per_device, mesh=mesh, in_specs=in_specs, out_specs=out_specs, check_vma=False
    )
```

```python
import jax
import jax.numpy as jnp
from jax import lax
from jax.sharding import PartitionSpec as P

ROPE = 64
VHEAD = 128
TOP = 8
BEAM = 4


def per_device(
    queries,
    latent_cache,
    new_key,
    parent_beam,
    value_up,
    out_proj,
    residual,
    expert_ids,
    route_gates,
    w_gate,
    w_up,
    w_down,
):
    rows = queries.shape[0]
    latent = value_up.shape[1]
    members = lax.axis_size("member")
    groups = lax.axis_size("group")
    experts = groups * members
    columns = out_proj.shape[1]
    scale = (VHEAD + ROPE) ** (-0.5)
    local_rows = jnp.arange(rows, dtype=jnp.int32)
    parent = local_rows // BEAM * BEAM + parent_beam
    keys = jnp.concatenate([jnp.take(latent_cache, parent, axis=0), new_key[:, None, :]], axis=1)
    chunks = 2
    step = rows // chunks
    pieces = []
    for c in range(chunks):
        asked = queries[c * step:(c + 1) * step]
        held = keys[c * step:(c + 1) * step]
        scores = jnp.einsum("rhw,rcw->rhc", asked, held, preferred_element_type=jnp.float32) * scale
        shifted = jnp.exp(scores - jnp.max(scores, axis=-1, keepdims=True))
        weights = (shifted / jnp.sum(shifted, axis=-1, keepdims=True)).astype(jnp.bfloat16)
        latent_out = jnp.einsum(
            "rhc,rcl->rhl", weights, held[:, :, :latent], preferred_element_type=jnp.float32
        ).astype(jnp.bfloat16)
        by_heads = lax.all_to_all(latent_out, "member", split_axis=1, concat_axis=0, tiled=True)
        per_head = jnp.einsum(
            "rhl,hlv->rhv", by_heads, value_up, preferred_element_type=jnp.float32
        ).astype(jnp.bfloat16)
        per_head = per_head.reshape(per_head.shape[0], per_head.shape[1] * per_head.shape[2])
        partial_sums = jnp.dot(
            lax.all_gather(per_head, "group", axis=0, tiled=True),
            out_proj,
            preferred_element_type=jnp.float32,
        )
        arrived_sums = lax.all_to_all(
            partial_sums.astype(jnp.bfloat16).reshape(members, -1, columns),
            "member",
            split_axis=0,
            concat_axis=0,
            tiled=True,
        )
        summed = jnp.sum(arrived_sums.astype(jnp.float32), axis=0)
        pieces.append(summed.reshape(-1, step, columns))
    attention = jnp.stack(pieces, axis=1).reshape(-1, columns)
    hidden_in = (residual.astype(jnp.float32) + attention).astype(jnp.bfloat16)
    block_rows = hidden_in.shape[0]
    capacity = max(2, 2 * rows * TOP // members)
    flat_ids = expert_ids.reshape(-1)
    onehot = (flat_ids[:, None] == jnp.arange(experts, dtype=jnp.int32)[None, :]).astype(jnp.int32)
    ranking = jnp.sum((jnp.cumsum(onehot, axis=0) - onehot) * onehot, axis=1)
    slot_index = flat_ids * capacity + ranking
    positions = jnp.arange(experts * capacity, dtype=jnp.int32)
    matches = (positions[:, None] == slot_index[None, :]).reshape(
        experts * capacity, block_rows, TOP
    )
    send_map = jnp.any(matches, axis=2).astype(jnp.bfloat16)
    outgoing = jnp.dot(send_map, hidden_in, preferred_element_type=jnp.float32).astype(jnp.bfloat16)
    arrived = lax.all_to_all(
        outgoing.reshape(experts, capacity, columns),
        ("group", "member"),
        split_axis=0,
        concat_axis=0,
        tiled=True,
    )
    expert_rows = (
        arrived.reshape(groups, members, capacity, columns)
        .transpose(1, 2, 0, 3)
        .reshape(members * capacity, groups * columns)
    )
    gate = jnp.dot(expert_rows, w_gate[0], preferred_element_type=jnp.float32)
    upper = jnp.dot(expert_rows, w_up[0], preferred_element_type=jnp.float32)
    inner = (jax.nn.silu(gate) * upper).astype(jnp.bfloat16)
    results = jnp.dot(inner, w_down[0], preferred_element_type=jnp.float32).astype(jnp.bfloat16)
    arranged = (
        results.reshape(members, capacity, groups, columns)
        .transpose(2, 0, 1, 3)
        .reshape(experts, capacity, columns)
    )
    returned = lax.all_to_all(
        arranged, ("group", "member"), split_axis=0, concat_axis=0, tiled=True
    )
    returned = returned.reshape(experts * capacity, columns)
    picked = returned[slot_index.reshape(block_rows, TOP)].astype(jnp.float32)
    mixed = jnp.sum(route_gates[:, :, None] * picked, axis=1)
    return (hidden_in.astype(jnp.float32) + mixed).astype(jnp.bfloat16)


def solution(mesh):
    in_specs = (
        P(("group", "member"), None, None),
        P(("group", "member"), None, None),
        P(("group", "member"), None),
        P(("group", "member")),
        P("member", None, None),
        P("member", "group"),
        P("member", "group"),
        P("member", None),
        P("member", None),
        P(("group", "member"), None, None),
        P(("group", "member"), None, None),
        P(("group", "member"), None, None),
    )
    out_specs = P("member", "group")
    return jax.shard_map(
        per_device, mesh=mesh, in_specs=in_specs, out_specs=out_specs, check_vma=False
    )
```

```python
import jax
import jax.numpy as jnp
from jax import lax
from jax.sharding import PartitionSpec as P

ROPE = 64
VHEAD = 128
TOP = 8
BEAM = 4


def per_device(
    queries,
    latent_cache,
    new_key,
    parent_beam,
    value_up,
    out_proj,
    residual,
    expert_ids,
    route_gates,
    w_gate,
    w_up,
    w_down,
):
    rows = queries.shape[0]
    latent = value_up.shape[1]
    members = lax.axis_size("member")
    groups = lax.axis_size("group")
    experts = groups * members
    columns = out_proj.shape[1]
    scale = (VHEAD + ROPE) ** (-0.5)
    local_rows = jnp.arange(rows, dtype=jnp.int32)
    parent = local_rows // BEAM * BEAM + parent_beam
    keys = jnp.concatenate([jnp.take(latent_cache, parent, axis=0), new_key[:, None, :]], axis=1)
    scores = jnp.einsum("rhw,rcw->rhc", queries, keys, preferred_element_type=jnp.float32) * scale
    shifted = jnp.exp(scores - jnp.max(scores, axis=-1, keepdims=True))
    weights = (shifted / jnp.sum(shifted, axis=-1, keepdims=True)).astype(jnp.bfloat16)
    latent_out = jnp.einsum(
        "rhc,rcl->rhl", weights, keys[:, :, :latent], preferred_element_type=jnp.float32
    ).astype(jnp.bfloat16)
    by_heads = lax.all_to_all(latent_out, "member", split_axis=1, concat_axis=0, tiled=True)
    per_head = jnp.einsum(
        "rhl,hlv->rhv", by_heads, value_up, preferred_element_type=jnp.float32
    ).astype(jnp.bfloat16)
    per_head = per_head.reshape(per_head.shape[0], per_head.shape[1] * per_head.shape[2])
    partial_sums = jnp.dot(
        lax.all_gather(per_head, "group", axis=0, tiled=True),
        out_proj,
        preferred_element_type=jnp.float32,
    )
    pieces = lax.all_to_all(
        partial_sums.astype(jnp.bfloat16).reshape(members, -1, columns),
        "member",
        split_axis=0,
        concat_axis=0,
        tiled=True,
    )
    attention = jnp.sum(pieces.astype(jnp.float32), axis=0)
    hidden_in = (residual.astype(jnp.float32) + attention).astype(jnp.bfloat16)
    block_rows = hidden_in.shape[0]
    capacity = max(2, 2 * rows * TOP // members)
    flat_ids = expert_ids.reshape(-1)
    onehot = (flat_ids[:, None] == jnp.arange(experts, dtype=jnp.int32)[None, :]).astype(jnp.int32)
    ranking = jnp.sum((jnp.cumsum(onehot, axis=0) - onehot) * onehot, axis=1)
    slot_index = flat_ids * capacity + ranking
    positions = jnp.arange(experts * capacity, dtype=jnp.int32)
    matches = (positions[:, None] == slot_index[None, :]).reshape(
        experts * capacity, block_rows, TOP
    )
    send_map = jnp.any(matches, axis=2).astype(jnp.bfloat16)
    outgoing = jnp.dot(send_map, hidden_in, preferred_element_type=jnp.float32).astype(jnp.bfloat16)
    arrived = lax.all_to_all(
        outgoing.reshape(experts, capacity, columns),
        ("group", "member"),
        split_axis=0,
        concat_axis=0,
        tiled=True,
    )
    arrived = arrived.reshape(groups, members * capacity, columns)
    gate = jnp.einsum(
        "gsc,gcf->sf", arrived, w_gate[0].reshape(groups, columns, -1),
        preferred_element_type=jnp.float32,
    )
    upper = jnp.einsum(
        "gsc,gcf->sf", arrived, w_up[0].reshape(groups, columns, -1),
        preferred_element_type=jnp.float32,
    )
    inner = (jax.nn.silu(gate) * upper).astype(jnp.bfloat16)
    results = jnp.einsum(
        "sf,fgc->gsc", inner, w_down[0].reshape(-1, groups, columns),
        preferred_element_type=jnp.float32,
    ).astype(jnp.bfloat16)
    returned = lax.all_to_all(
        results.reshape(experts, capacity, columns),
        ("group", "member"),
        split_axis=0,
        concat_axis=0,
        tiled=True,
    )
    returned = returned.reshape(experts * capacity, columns)
    slots = slot_index.reshape(block_rows, TOP)
    gate_hi = route_gates.astype(jnp.bfloat16)
    gate_lo = (route_gates - gate_hi.astype(jnp.float32)).astype(jnp.bfloat16)
    hit = slots[:, :, None] == positions[None, None, :]
    zero = jnp.zeros((), jnp.bfloat16)
    map_hi = jnp.sum(jnp.where(hit, gate_hi[:, :, None], zero), axis=1)
    map_lo = jnp.sum(jnp.where(hit, gate_lo[:, :, None], zero), axis=1)
    mixed = jnp.dot(map_hi, returned, preferred_element_type=jnp.float32) + jnp.dot(
        map_lo, returned, preferred_element_type=jnp.float32
    )
    return (hidden_in.astype(jnp.float32) + mixed).astype(jnp.bfloat16)


def solution(mesh):
    in_specs = (
        P(("group", "member"), None, None),
        P(("group", "member"), None, None),
        P(("group", "member"), None),
        P(("group", "member")),
        P("member", None, None),
        P("member", "group"),
        P("member", "group"),
        P("member", None),
        P("member", None),
        P(("group", "member"), None, None),
        P(("group", "member"), None, None),
        P(("group", "member"), None, None),
    )
    out_specs = P("member", "group")
    return jax.shard_map(
        per_device, mesh=mesh, in_specs=in_specs, out_specs=out_specs, check_vma=False
    )
```

```python
import jax
import jax.numpy as jnp
from jax import lax
from jax.sharding import PartitionSpec as P

ROPE = 64
VHEAD = 128
TOP = 8
BEAM = 4


def per_device(
    queries,
    latent_cache,
    new_key,
    parent_beam,
    value_up,
    out_proj,
    residual,
    expert_ids,
    route_gates,
    w_gate,
    w_up,
    w_down,
):
    rows = queries.shape[0]
    latent = value_up.shape[1]
    members = lax.axis_size("member")
    groups = lax.axis_size(("gy", "gc"))
    experts = groups * members
    columns = out_proj.shape[1]
    scale = (VHEAD + ROPE) ** (-0.5)
    local_rows = jnp.arange(rows, dtype=jnp.int32)
    parent = local_rows // BEAM * BEAM + parent_beam
    keys = jnp.concatenate([jnp.take(latent_cache, parent, axis=0), new_key[:, None, :]], axis=1)
    scores = jnp.einsum("rhw,rcw->rhc", queries, keys, preferred_element_type=jnp.float32) * scale
    shifted = jnp.exp(scores - jnp.max(scores, axis=-1, keepdims=True))
    weights = (shifted / jnp.sum(shifted, axis=-1, keepdims=True)).astype(jnp.bfloat16)
    latent_out = jnp.einsum(
        "rhc,rcl->rhl", weights, keys[:, :, :latent], preferred_element_type=jnp.float32
    ).astype(jnp.bfloat16)
    by_heads = lax.all_to_all(latent_out, "member", split_axis=1, concat_axis=0, tiled=True)
    per_head = jnp.einsum(
        "rhl,hlv->rhv", by_heads, value_up, preferred_element_type=jnp.float32
    ).astype(jnp.bfloat16)
    per_head = per_head.reshape(per_head.shape[0], per_head.shape[1] * per_head.shape[2])
    along_y = lax.all_gather(per_head, "gy", axis=0, tiled=True)
    both_cores = lax.all_gather(along_y, "gc", axis=0, tiled=True)
    cores = lax.axis_size("gc")
    gathered = (
        both_cores.reshape(cores, groups // cores, -1, per_head.shape[1])
        .transpose(1, 0, 2, 3)
        .reshape(-1, per_head.shape[1])
    )
    partial_sums = jnp.dot(gathered, out_proj, preferred_element_type=jnp.float32)
    pieces = lax.all_to_all(
        partial_sums.astype(jnp.bfloat16).reshape(members, -1, columns),
        "member",
        split_axis=0,
        concat_axis=0,
        tiled=True,
    )
    attention = jnp.sum(pieces.astype(jnp.float32), axis=0)
    hidden_in = (residual.astype(jnp.float32) + attention).astype(jnp.bfloat16)
    block_rows = hidden_in.shape[0]
    capacity = max(2, 2 * rows * TOP // members)
    flat_ids = expert_ids.reshape(-1)
    onehot = (flat_ids[:, None] == jnp.arange(experts, dtype=jnp.int32)[None, :]).astype(jnp.int32)
    ranking = jnp.sum((jnp.cumsum(onehot, axis=0) - onehot) * onehot, axis=1)
    slot_index = flat_ids * capacity + ranking
    positions = jnp.arange(experts * capacity, dtype=jnp.int32)
    matches = (positions[:, None] == slot_index[None, :]).reshape(
        experts * capacity, block_rows, TOP
    )
    send_map = jnp.any(matches, axis=2).astype(jnp.bfloat16)
    outgoing = jnp.dot(send_map, hidden_in, preferred_element_type=jnp.float32).astype(jnp.bfloat16)
    arrived = lax.all_to_all(
        outgoing.reshape(experts, capacity, columns),
        ("gy", "gc", "member"),
        split_axis=0,
        concat_axis=0,
        tiled=True,
    )
    arrived = arrived.reshape(groups, members * capacity, columns)
    gate = jnp.einsum(
        "gsc,gcf->sf", arrived, w_gate[0].reshape(groups, columns, -1),
        preferred_element_type=jnp.float32,
    )
    upper = jnp.einsum(
        "gsc,gcf->sf", arrived, w_up[0].reshape(groups, columns, -1),
        preferred_element_type=jnp.float32,
    )
    inner = (jax.nn.silu(gate) * upper).astype(jnp.bfloat16)
    results = jnp.einsum(
        "sf,fgc->gsc", inner, w_down[0].reshape(-1, groups, columns),
        preferred_element_type=jnp.float32,
    ).astype(jnp.bfloat16)
    returned = lax.all_to_all(
        results.reshape(experts, capacity, columns),
        ("gy", "gc", "member"),
        split_axis=0,
        concat_axis=0,
        tiled=True,
    )
    returned = returned.reshape(experts * capacity, columns)
    slots = slot_index.reshape(block_rows, TOP)
    gate_hi = route_gates.astype(jnp.bfloat16)
    gate_lo = (route_gates - gate_hi.astype(jnp.float32)).astype(jnp.bfloat16)
    hit = slots[:, :, None] == positions[None, None, :]
    zero = jnp.zeros((), jnp.bfloat16)
    map_hi = jnp.sum(jnp.where(hit, gate_hi[:, :, None], zero), axis=1)
    map_lo = jnp.sum(jnp.where(hit, gate_lo[:, :, None], zero), axis=1)
    mixed = jnp.dot(map_hi, returned, preferred_element_type=jnp.float32) + jnp.dot(
        map_lo, returned, preferred_element_type=jnp.float32
    )
    return (hidden_in.astype(jnp.float32) + mixed).astype(jnp.bfloat16)


def solution(mesh):
    shape = mesh.devices.shape
    split = jax.sharding.Mesh(mesh.devices.reshape(shape[0] // 2, 2, shape[1]), ("gy", "gc", "member"))
    group = ("gy", "gc")
    everyone = ("gy", "gc", "member")
    in_specs = (
        P(everyone, None, None),
        P(everyone, None, None),
        P(everyone, None),
        P(everyone),
        P("member", None, None),
        P("member", group),
        P("member", group),
        P("member", None),
        P("member", None),
        P(everyone, None, None),
        P(everyone, None, None),
        P(everyone, None, None),
    )
    out_specs = P("member", group)
    return jax.shard_map(
        per_device, mesh=split, in_specs=in_specs, out_specs=out_specs, check_vma=False
    )
```

```python
import jax
import jax.numpy as jnp
from jax import lax
from jax.sharding import PartitionSpec as P

ROPE = 64
VHEAD = 128
TOP = 8
BEAM = 4


def per_device(
    queries,
    latent_cache,
    new_key,
    parent_beam,
    value_up,
    out_proj,
    residual,
    expert_ids,
    route_gates,
    w_gate,
    w_up,
    w_down,
):
    rows = queries.shape[0]
    latent = value_up.shape[1]
    members = lax.axis_size("member")
    groups = lax.axis_size("group")
    experts = groups * members
    columns = out_proj.shape[1]
    scale = (VHEAD + ROPE) ** (-0.5)
    local_rows = jnp.arange(rows, dtype=jnp.int32)
    parent = local_rows // BEAM * BEAM + parent_beam
    keys = jnp.concatenate([jnp.take(latent_cache, parent, axis=0), new_key[:, None, :]], axis=1)
    scores = jnp.einsum("rhw,rcw->rhc", queries, keys, preferred_element_type=jnp.float32) * scale
    shifted = jnp.exp(scores - jnp.max(scores, axis=-1, keepdims=True))
    weights = (shifted / jnp.sum(shifted, axis=-1, keepdims=True)).astype(jnp.bfloat16)
    latent_out = jnp.einsum(
        "rhc,rcl->rhl", weights, keys[:, :, :latent], preferred_element_type=jnp.float32
    ).astype(jnp.bfloat16)
    by_heads = lax.all_to_all(latent_out, "member", split_axis=1, concat_axis=0, tiled=True)
    per_head = jnp.einsum(
        "rhl,hlv->rhv", by_heads, value_up, preferred_element_type=jnp.float32
    ).astype(jnp.bfloat16)
    per_head = per_head.reshape(per_head.shape[0], per_head.shape[1] * per_head.shape[2])
    weights_all = lax.all_gather(out_proj, "group", axis=1, tiled=True)
    partial_sums = jnp.dot(per_head, weights_all, preferred_element_type=jnp.float32)
    halves = per_head.shape[0] // residual.shape[0]
    pieces = (
        partial_sums.astype(jnp.bfloat16)
        .reshape(halves, -1, groups, columns)
        .transpose(0, 2, 1, 3)
        .reshape(members, -1, columns)
    )
    pieces = lax.all_to_all(pieces, "member", split_axis=0, concat_axis=0, tiled=True)
    summed = jnp.sum(pieces.astype(jnp.float32), axis=0)
    owner = [
        (g * members + m, (m % groups) * members + (m // groups) + halves * g)
        for g in range(groups)
        for m in range(members)
    ]
    attention = lax.ppermute(summed, ("group", "member"), perm=owner)
    hidden_in = (residual.astype(jnp.float32) + attention).astype(jnp.bfloat16)
    block_rows = hidden_in.shape[0]
    capacity = max(2, 2 * rows * TOP // members)
    flat_ids = expert_ids.reshape(-1)
    onehot = (flat_ids[:, None] == jnp.arange(experts, dtype=jnp.int32)[None, :]).astype(jnp.int32)
    ranking = jnp.sum((jnp.cumsum(onehot, axis=0) - onehot) * onehot, axis=1)
    slot_index = flat_ids * capacity + ranking
    positions = jnp.arange(experts * capacity, dtype=jnp.int32)
    matches = (positions[:, None] == slot_index[None, :]).reshape(
        experts * capacity, block_rows, TOP
    )
    send_map = jnp.any(matches, axis=2).astype(jnp.bfloat16)
    outgoing = jnp.dot(send_map, hidden_in, preferred_element_type=jnp.float32).astype(jnp.bfloat16)
    arrived = lax.all_to_all(
        outgoing.reshape(experts, capacity, columns),
        ("group", "member"),
        split_axis=0,
        concat_axis=0,
        tiled=True,
    )
    arrived = arrived.reshape(groups, members * capacity, columns)
    gate = jnp.einsum(
        "gsc,gcf->sf", arrived, w_gate[0].reshape(groups, columns, -1),
        preferred_element_type=jnp.float32,
    )
    upper = jnp.einsum(
        "gsc,gcf->sf", arrived, w_up[0].reshape(groups, columns, -1),
        preferred_element_type=jnp.float32,
    )
    inner = (jax.nn.silu(gate) * upper).astype(jnp.bfloat16)
    results = jnp.einsum(
        "sf,fgc->gsc", inner, w_down[0].reshape(-1, groups, columns),
        preferred_element_type=jnp.float32,
    ).astype(jnp.bfloat16)
    returned = lax.all_to_all(
        results.reshape(experts, capacity, columns),
        ("group", "member"),
        split_axis=0,
        concat_axis=0,
        tiled=True,
    )
    returned = returned.reshape(experts * capacity, columns)
    slots = slot_index.reshape(block_rows, TOP)
    gate_hi = route_gates.astype(jnp.bfloat16)
    gate_lo = (route_gates - gate_hi.astype(jnp.float32)).astype(jnp.bfloat16)
    hit = slots[:, :, None] == positions[None, None, :]
    zero = jnp.zeros((), jnp.bfloat16)
    map_hi = jnp.sum(jnp.where(hit, gate_hi[:, :, None], zero), axis=1)
    map_lo = jnp.sum(jnp.where(hit, gate_lo[:, :, None], zero), axis=1)
    mixed = jnp.dot(map_hi, returned, preferred_element_type=jnp.float32) + jnp.dot(
        map_lo, returned, preferred_element_type=jnp.float32
    )
    return (hidden_in.astype(jnp.float32) + mixed).astype(jnp.bfloat16)


def solution(mesh):
    in_specs = (
        P(("group", "member"), None, None),
        P(("group", "member"), None, None),
        P(("group", "member"), None),
        P(("group", "member")),
        P("member", None, None),
        P("member", "group"),
        P("member", "group"),
        P("member", None),
        P("member", None),
        P(("group", "member"), None, None),
        P(("group", "member"), None, None),
        P(("group", "member"), None, None),
    )
    out_specs = P("member", "group")
    return jax.shard_map(
        per_device, mesh=mesh, in_specs=in_specs, out_specs=out_specs, check_vma=False
    )
```

```python
import jax
import jax.numpy as jnp
from jax import lax
from jax.sharding import PartitionSpec as P

ROPE = 64
VHEAD = 128
TOP = 8
BEAM = 4


def per_device(
    queries,
    latent_cache,
    new_key,
    parent_beam,
    value_up,
    out_proj,
    residual,
    expert_ids,
    route_gates,
    w_gate,
    w_up,
    w_down,
):
    rows = queries.shape[0]
    latent = value_up.shape[1]
    members = lax.axis_size("member")
    groups = lax.axis_size("group")
    experts = groups * members
    columns = out_proj.shape[1]
    scale = (VHEAD + ROPE) ** (-0.5)
    local_rows = jnp.arange(rows, dtype=jnp.int32)
    parent = local_rows // BEAM * BEAM + parent_beam
    keys = jnp.concatenate([jnp.take(latent_cache, parent, axis=0), new_key[:, None, :]], axis=1)
    scores = jnp.einsum("rhw,rcw->rhc", queries, keys, preferred_element_type=jnp.float32) * scale
    shifted = jnp.exp(scores - jnp.max(scores, axis=-1, keepdims=True))
    weights = (shifted / jnp.sum(shifted, axis=-1, keepdims=True)).astype(jnp.bfloat16)
    latent_out = jnp.einsum(
        "rhc,rcl->rhl", weights, keys[:, :, :latent], preferred_element_type=jnp.float32
    ).astype(jnp.bfloat16)
    by_heads = lax.all_to_all(latent_out, "member", split_axis=1, concat_axis=0, tiled=True)
    per_head = jnp.einsum(
        "rhl,hlv->rhv", by_heads, value_up, preferred_element_type=jnp.float32
    ).astype(jnp.bfloat16)
    per_head = per_head.reshape(per_head.shape[0], per_head.shape[1] * per_head.shape[2])
    weights_all = lax.all_gather(out_proj, "group", axis=0, tiled=False)
    halves = per_head.shape[0] // residual.shape[0]
    pieces = jnp.einsum(
        "irk,ckn->icrn",
        per_head.reshape(halves, -1, per_head.shape[1]),
        weights_all,
        preferred_element_type=jnp.float32,
    ).astype(jnp.bfloat16).reshape(members, -1, columns)
    pieces = lax.all_to_all(pieces, "member", split_axis=0, concat_axis=0, tiled=True)
    summed = jnp.sum(pieces.astype(jnp.float32), axis=0)
    owner = [
        (g * members + m, (m % groups) * members + (m // groups) + halves * g)
        for g in range(groups)
        for m in range(members)
    ]
    attention = lax.ppermute(summed, ("group", "member"), perm=owner)
    hidden_in = (residual.astype(jnp.float32) + attention).astype(jnp.bfloat16)
    block_rows = hidden_in.shape[0]
    capacity = max(2, 2 * rows * TOP // members)
    flat_ids = expert_ids.reshape(-1)
    onehot = (flat_ids[:, None] == jnp.arange(experts, dtype=jnp.int32)[None, :]).astype(jnp.int32)
    ranking = jnp.sum((jnp.cumsum(onehot, axis=0) - onehot) * onehot, axis=1)
    slot_index = flat_ids * capacity + ranking
    positions = jnp.arange(experts * capacity, dtype=jnp.int32)
    matches = (positions[:, None] == slot_index[None, :]).reshape(
        experts * capacity, block_rows, TOP
    )
    send_map = jnp.any(matches, axis=2).astype(jnp.bfloat16)
    outgoing = jnp.dot(send_map, hidden_in, preferred_element_type=jnp.float32).astype(jnp.bfloat16)
    arrived = lax.all_to_all(
        outgoing.reshape(experts, capacity, columns),
        ("group", "member"),
        split_axis=0,
        concat_axis=0,
        tiled=True,
    )
    arrived = arrived.reshape(groups, members * capacity, columns)
    gate = jnp.einsum(
        "gsc,gcf->sf", arrived, w_gate[0].reshape(groups, columns, -1),
        preferred_element_type=jnp.float32,
    )
    upper = jnp.einsum(
        "gsc,gcf->sf", arrived, w_up[0].reshape(groups, columns, -1),
        preferred_element_type=jnp.float32,
    )
    inner = (jax.nn.silu(gate) * upper).astype(jnp.bfloat16)
    results = jnp.einsum(
        "sf,fgc->gsc", inner, w_down[0].reshape(-1, groups, columns),
        preferred_element_type=jnp.float32,
    ).astype(jnp.bfloat16)
    returned = lax.all_to_all(
        results.reshape(experts, capacity, columns),
        ("group", "member"),
        split_axis=0,
        concat_axis=0,
        tiled=True,
    )
    returned = returned.reshape(experts * capacity, columns)
    slots = slot_index.reshape(block_rows, TOP)
    gate_hi = route_gates.astype(jnp.bfloat16)
    gate_lo = (route_gates - gate_hi.astype(jnp.float32)).astype(jnp.bfloat16)
    hit = slots[:, :, None] == positions[None, None, :]
    zero = jnp.zeros((), jnp.bfloat16)
    map_hi = jnp.sum(jnp.where(hit, gate_hi[:, :, None], zero), axis=1)
    map_lo = jnp.sum(jnp.where(hit, gate_lo[:, :, None], zero), axis=1)
    mixed = jnp.dot(map_hi, returned, preferred_element_type=jnp.float32) + jnp.dot(
        map_lo, returned, preferred_element_type=jnp.float32
    )
    return (hidden_in.astype(jnp.float32) + mixed).astype(jnp.bfloat16)


def solution(mesh):
    in_specs = (
        P(("group", "member"), None, None),
        P(("group", "member"), None, None),
        P(("group", "member"), None),
        P(("group", "member")),
        P("member", None, None),
        P("member", "group"),
        P("member", "group"),
        P("member", None),
        P("member", None),
        P(("group", "member"), None, None),
        P(("group", "member"), None, None),
        P(("group", "member"), None, None),
    )
    out_specs = P("member", "group")
    return jax.shard_map(
        per_device, mesh=mesh, in_specs=in_specs, out_specs=out_specs, check_vma=False
    )
```

```python
import jax
import jax.numpy as jnp
from jax import lax
from jax.sharding import PartitionSpec as P

ROPE = 64
VHEAD = 128
TOP = 8
BEAM = 4


def per_device(
    queries,
    latent_cache,
    new_key,
    parent_beam,
    value_up,
    out_proj,
    residual,
    expert_ids,
    route_gates,
    w_gate,
    w_up,
    w_down,
):
    rows = queries.shape[0]
    latent = value_up.shape[1]
    members = lax.axis_size("member")
    groups = lax.axis_size("group")
    experts = groups * members
    columns = out_proj.shape[1]
    scale = (VHEAD + ROPE) ** (-0.5)
    context = latent_cache.shape[1]
    width = latent_cache.shape[2]
    beams = latent_cache.reshape(rows // BEAM, BEAM, context, width)
    chosen = parent_beam.reshape(rows // BEAM, BEAM, 1, 1)
    held = jnp.broadcast_to(beams[:, BEAM - 1 : BEAM], beams.shape)
    for beam in range(BEAM - 2, -1, -1):
        held = jnp.where(chosen == beam, beams[:, beam : beam + 1], held)
    held = held.reshape(rows, context, width)
    scores = jnp.einsum("rhw,rcw->rhc", queries, held, preferred_element_type=jnp.float32) * scale
    own = jnp.einsum("rhw,rw->rh", queries, new_key, preferred_element_type=jnp.float32) * scale
    top = jnp.maximum(jnp.max(scores, axis=-1), own)
    shifted = jnp.exp(scores - top[:, :, None])
    own_shifted = jnp.exp(own - top)
    total = jnp.sum(shifted, axis=-1) + own_shifted
    weights = (shifted / total[:, :, None]).astype(jnp.bfloat16)
    own_weight = (own_shifted / total).astype(jnp.bfloat16)
    mixed_cache = jnp.einsum(
        "rhc,rcl->rhl", weights, held[:, :, :latent], preferred_element_type=jnp.float32
    )
    mixed_new = own_weight.astype(jnp.float32)[:, :, None] * new_key[:, None, :latent].astype(jnp.float32)
    latent_out = (mixed_cache + mixed_new).astype(jnp.bfloat16)
    by_heads = lax.all_to_all(latent_out, "member", split_axis=1, concat_axis=0, tiled=True)
    per_head = jnp.einsum(
        "rhl,hlv->rhv", by_heads, value_up, preferred_element_type=jnp.float32
    ).astype(jnp.bfloat16)
    per_head = per_head.reshape(per_head.shape[0], per_head.shape[1] * per_head.shape[2])
    weights_all = lax.all_gather(out_proj, "group", axis=0, tiled=False)
    halves = per_head.shape[0] // residual.shape[0]
    pieces = jnp.einsum(
        "irk,ckn->icrn",
        per_head.reshape(halves, -1, per_head.shape[1]),
        weights_all,
        preferred_element_type=jnp.float32,
    ).astype(jnp.bfloat16).reshape(members, -1, columns)
    pieces = lax.all_to_all(pieces, "member", split_axis=0, concat_axis=0, tiled=True)
    summed = jnp.sum(pieces.astype(jnp.float32), axis=0)
    owner = [
        (g * members + m, (m % groups) * members + (m // groups) + halves * g)
        for g in range(groups)
        for m in range(members)
    ]
    attention = lax.ppermute(summed, ("group", "member"), perm=owner)
    hidden_in = (residual.astype(jnp.float32) + attention).astype(jnp.bfloat16)
    block_rows = hidden_in.shape[0]
    capacity = max(2, 2 * rows * TOP // members)
    flat_ids = expert_ids.reshape(-1)
    onehot = (flat_ids[:, None] == jnp.arange(experts, dtype=jnp.int32)[None, :]).astype(jnp.int32)
    ranking = jnp.sum((jnp.cumsum(onehot, axis=0) - onehot) * onehot, axis=1)
    slot_index = flat_ids * capacity + ranking
    positions = jnp.arange(experts * capacity, dtype=jnp.int32)
    matches = (positions[:, None] == slot_index[None, :]).reshape(
        experts * capacity, block_rows, TOP
    )
    send_map = jnp.any(matches, axis=2).astype(jnp.bfloat16)
    outgoing = jnp.dot(send_map, hidden_in, preferred_element_type=jnp.float32).astype(jnp.bfloat16)
    arrived = lax.all_to_all(
        outgoing.reshape(experts, capacity, columns),
        ("group", "member"),
        split_axis=0,
        concat_axis=0,
        tiled=True,
    )
    arrived = arrived.reshape(groups, members * capacity, columns)
    gate = jnp.einsum(
        "gsc,gcf->sf", arrived, w_gate[0].reshape(groups, columns, -1),
        preferred_element_type=jnp.float32,
    )
    upper = jnp.einsum(
        "gsc,gcf->sf", arrived, w_up[0].reshape(groups, columns, -1),
        preferred_element_type=jnp.float32,
    )
    inner = (jax.nn.silu(gate) * upper).astype(jnp.bfloat16)
    results = jnp.einsum(
        "sf,fgc->gsc", inner, w_down[0].reshape(-1, groups, columns),
        preferred_element_type=jnp.float32,
    ).astype(jnp.bfloat16)
    returned = lax.all_to_all(
        results.reshape(experts, capacity, columns),
        ("group", "member"),
        split_axis=0,
        concat_axis=0,
        tiled=True,
    )
    returned = returned.reshape(experts * capacity, columns)
    slots = slot_index.reshape(block_rows, TOP)
    gate_hi = route_gates.astype(jnp.bfloat16)
    gate_lo = (route_gates - gate_hi.astype(jnp.float32)).astype(jnp.bfloat16)
    hit = slots[:, :, None] == positions[None, None, :]
    zero = jnp.zeros((), jnp.bfloat16)
    map_hi = jnp.sum(jnp.where(hit, gate_hi[:, :, None], zero), axis=1)
    map_lo = jnp.sum(jnp.where(hit, gate_lo[:, :, None], zero), axis=1)
    mixed = jnp.dot(map_hi, returned, preferred_element_type=jnp.float32) + jnp.dot(
        map_lo, returned, preferred_element_type=jnp.float32
    )
    return (hidden_in.astype(jnp.float32) + mixed).astype(jnp.bfloat16)


def solution(mesh):
    in_specs = (
        P(("group", "member"), None, None),
        P(("group", "member"), None, None),
        P(("group", "member"), None),
        P(("group", "member")),
        P("member", None, None),
        P("member", "group"),
        P("member", "group"),
        P("member", None),
        P("member", None),
        P(("group", "member"), None, None),
        P(("group", "member"), None, None),
        P(("group", "member"), None, None),
    )
    out_specs = P("member", "group")
    return jax.shard_map(
        per_device, mesh=mesh, in_specs=in_specs, out_specs=out_specs, check_vma=False
    )
```

```python
import jax
import jax.numpy as jnp
from jax import lax
from jax.sharding import PartitionSpec as P

ROPE = 64
VHEAD = 128
TOP = 8
BEAM = 4


def per_device(
    queries,
    latent_cache,
    new_key,
    parent_beam,
    value_up,
    out_proj,
    residual,
    expert_ids,
    route_gates,
    w_gate,
    w_up,
    w_down,
):
    rows = queries.shape[0]
    latent = value_up.shape[1]
    members = lax.axis_size("member")
    groups = lax.axis_size("group")
    experts = groups * members
    columns = out_proj.shape[1]
    scale = (VHEAD + ROPE) ** (-0.5)
    context = latent_cache.shape[1]
    width = latent_cache.shape[2]
    beams = latent_cache.reshape(rows // BEAM, BEAM, context, width)
    chosen = parent_beam.reshape(rows // BEAM, BEAM, 1, 1)
    held = jnp.broadcast_to(beams[:, BEAM - 1 : BEAM], beams.shape)
    for beam in range(BEAM - 2, -1, -1):
        held = jnp.where(chosen == beam, beams[:, beam : beam + 1], held)
    held = held.reshape(rows, context, width)
    scores = jnp.einsum("rhw,rcw->rhc", queries, held, preferred_element_type=jnp.float32) * scale
    own = jnp.einsum("rhw,rw->rh", queries, new_key, preferred_element_type=jnp.float32) * scale
    top = jnp.maximum(jnp.max(scores, axis=-1), own)
    shifted = jnp.exp(scores - top[:, :, None])
    own_shifted = jnp.exp(own - top)
    total = jnp.sum(shifted, axis=-1) + own_shifted
    weights = (shifted / total[:, :, None]).astype(jnp.bfloat16)
    own_weight = (own_shifted / total).astype(jnp.bfloat16)
    mixed_cache = jnp.einsum(
        "rhc,rcl->rhl", weights, held[:, :, :latent], preferred_element_type=jnp.float32
    )
    mixed_new = own_weight.astype(jnp.float32)[:, :, None] * new_key[:, None, :latent].astype(jnp.float32)
    latent_out = (mixed_cache + mixed_new).astype(jnp.bfloat16)
    by_heads = lax.all_to_all(latent_out, "member", split_axis=1, concat_axis=0, tiled=True)
    per_head = jnp.einsum(
        "rhl,hlv->rhv", by_heads, value_up, preferred_element_type=jnp.float32
    ).astype(jnp.bfloat16)
    per_head = per_head.reshape(per_head.shape[0], per_head.shape[1] * per_head.shape[2])
    weights_all = lax.all_gather(out_proj, "group", axis=0, tiled=False)
    halves = per_head.shape[0] // residual.shape[0]
    pieces = jnp.einsum(
        "irk,ckn->icrn",
        per_head.reshape(halves, -1, per_head.shape[1]),
        weights_all,
        preferred_element_type=jnp.float32,
    ).astype(jnp.bfloat16).reshape(members, -1, columns)
    pieces = lax.all_to_all(pieces, "member", split_axis=0, concat_axis=0, tiled=True)
    block_rows = residual.shape[0]
    capacity = max(2, 2 * rows * TOP // members)
    flat_ids = expert_ids.reshape(-1)
    onehot = (flat_ids[:, None] == jnp.arange(experts, dtype=jnp.int32)[None, :]).astype(jnp.int32)
    ranking = jnp.sum((jnp.cumsum(onehot, axis=0) - onehot) * onehot, axis=1)
    slot_index = flat_ids * capacity + ranking
    positions = jnp.arange(experts * capacity, dtype=jnp.int32)
    matches = (positions[:, None] == slot_index[None, :]).reshape(
        experts * capacity, block_rows, TOP
    )
    send_map = jnp.any(matches, axis=2).astype(jnp.bfloat16)
    pieces, send_map, slot_index = lax.optimization_barrier((pieces, send_map, slot_index))
    summed = jnp.sum(pieces.astype(jnp.float32), axis=0)
    owner = [
        (g * members + m, (m % groups) * members + (m // groups) + halves * g)
        for g in range(groups)
        for m in range(members)
    ]
    attention = lax.ppermute(summed, ("group", "member"), perm=owner)
    hidden_in = (residual.astype(jnp.float32) + attention).astype(jnp.bfloat16)
    outgoing = jnp.dot(send_map, hidden_in, preferred_element_type=jnp.float32).astype(jnp.bfloat16)
    arrived = lax.all_to_all(
        outgoing.reshape(experts, capacity, columns),
        ("group", "member"),
        split_axis=0,
        concat_axis=0,
        tiled=True,
    )
    arrived = arrived.reshape(groups, members * capacity, columns)
    gate = jnp.einsum(
        "gsc,gcf->sf", arrived, w_gate[0].reshape(groups, columns, -1),
        preferred_element_type=jnp.float32,
    )
    upper = jnp.einsum(
        "gsc,gcf->sf", arrived, w_up[0].reshape(groups, columns, -1),
        preferred_element_type=jnp.float32,
    )
    inner = (jax.nn.silu(gate) * upper).astype(jnp.bfloat16)
    results = jnp.einsum(
        "sf,fgc->gsc", inner, w_down[0].reshape(-1, groups, columns),
        preferred_element_type=jnp.float32,
    ).astype(jnp.bfloat16)
    returned = lax.all_to_all(
        results.reshape(experts, capacity, columns),
        ("group", "member"),
        split_axis=0,
        concat_axis=0,
        tiled=True,
    )
    returned = returned.reshape(experts * capacity, columns)
    slots = slot_index.reshape(block_rows, TOP)
    gate_hi = route_gates.astype(jnp.bfloat16)
    gate_lo = (route_gates - gate_hi.astype(jnp.float32)).astype(jnp.bfloat16)
    hit = slots[:, :, None] == positions[None, None, :]
    zero = jnp.zeros((), jnp.bfloat16)
    map_hi = jnp.sum(jnp.where(hit, gate_hi[:, :, None], zero), axis=1)
    map_lo = jnp.sum(jnp.where(hit, gate_lo[:, :, None], zero), axis=1)
    mixed = jnp.dot(map_hi, returned, preferred_element_type=jnp.float32) + jnp.dot(
        map_lo, returned, preferred_element_type=jnp.float32
    )
    return (hidden_in.astype(jnp.float32) + mixed).astype(jnp.bfloat16)


def solution(mesh):
    in_specs = (
        P(("group", "member"), None, None),
        P(("group", "member"), None, None),
        P(("group", "member"), None),
        P(("group", "member")),
        P("member", None, None),
        P("member", "group"),
        P("member", "group"),
        P("member", None),
        P("member", None),
        P(("group", "member"), None, None),
        P(("group", "member"), None, None),
        P(("group", "member"), None, None),
    )
    out_specs = P("member", "group")
    return jax.shard_map(
        per_device, mesh=mesh, in_specs=in_specs, out_specs=out_specs, check_vma=False
    )
```

```python
import jax
import jax.numpy as jnp
from jax import lax
from jax.sharding import PartitionSpec as P

ROPE = 64
VHEAD = 128
TOP = 8
BEAM = 4


def per_device(
    queries,
    latent_cache,
    new_key,
    parent_beam,
    value_up,
    out_proj,
    residual,
    expert_ids,
    route_gates,
    w_gate,
    w_up,
    w_down,
):
    rows = queries.shape[0]
    latent = value_up.shape[1]
    members = lax.axis_size("member")
    groups = lax.axis_size("group")
    experts = groups * members
    columns = out_proj.shape[1]
    scale = (VHEAD + ROPE) ** (-0.5)
    context = latent_cache.shape[1]
    width = latent_cache.shape[2]
    beams = latent_cache.reshape(rows // BEAM, BEAM, context, width)
    chosen = parent_beam.reshape(rows // BEAM, BEAM, 1, 1)
    held = jnp.broadcast_to(beams[:, BEAM - 1 : BEAM], beams.shape)
    for beam in range(BEAM - 2, -1, -1):
        held = jnp.where(chosen == beam, beams[:, beam : beam + 1], held)
    held = held.reshape(rows, context, width)
    scores = jnp.einsum("rhw,rcw->rhc", queries, held, preferred_element_type=jnp.float32) * scale
    own = jnp.einsum("rhw,rw->rh", queries, new_key, preferred_element_type=jnp.float32) * scale
    top = jnp.maximum(jnp.max(scores, axis=-1), own)
    shifted = jnp.exp(scores - top[:, :, None])
    own_shifted = jnp.exp(own - top)
    total = jnp.sum(shifted, axis=-1) + own_shifted
    weights = (shifted / total[:, :, None]).astype(jnp.bfloat16)
    own_weight = (own_shifted / total).astype(jnp.bfloat16)
    mixed_cache = jnp.einsum(
        "rhc,rcl->rhl", weights, held[:, :, :latent], preferred_element_type=jnp.float32
    )
    mixed_new = own_weight.astype(jnp.float32)[:, :, None] * new_key[:, None, :latent].astype(jnp.float32)
    latent_out = (mixed_cache + mixed_new).astype(jnp.bfloat16)
    by_heads = lax.all_to_all(latent_out, "member", split_axis=1, concat_axis=0, tiled=True)
    per_head = jnp.einsum(
        "rhl,hlv->rhv", by_heads, value_up, preferred_element_type=jnp.float32
    ).astype(jnp.bfloat16)
    per_head = per_head.reshape(per_head.shape[0], per_head.shape[1] * per_head.shape[2])
    weights_all = lax.all_gather(out_proj, "group", axis=0, tiled=False)
    halves = per_head.shape[0] // residual.shape[0]
    pieces = jnp.einsum(
        "irk,ckn->icrn",
        per_head.reshape(halves, -1, per_head.shape[1]),
        weights_all,
        preferred_element_type=jnp.float32,
    ).astype(jnp.bfloat16).reshape(members, -1, columns)
    pieces = lax.all_to_all(pieces, "member", split_axis=0, concat_axis=0, tiled=True)
    block_rows = residual.shape[0]
    capacity = max(2, 2 * rows * TOP // members)
    positions = jnp.arange(experts * capacity, dtype=jnp.int32)
    to_owner = [
        (g * members + m, (m % groups) * members + (m // groups) + halves * g)
        for g in range(groups)
        for m in range(members)
    ]
    to_holder = [(b, a) for a, b in to_owner]
    everyone = ("group", "member")
    held_residual = lax.ppermute(residual, everyone, perm=to_holder)
    held_ids = lax.ppermute(expert_ids, everyone, perm=to_holder)

    def route(ids):
        flat_ids = ids.reshape(-1)
        onehot = (flat_ids[:, None] == jnp.arange(experts, dtype=jnp.int32)[None, :]).astype(jnp.int32)
        ranking = jnp.sum((jnp.cumsum(onehot, axis=0) - onehot) * onehot, axis=1)
        return flat_ids * capacity + ranking

    held_slots = route(held_ids)
    matches = (positions[:, None] == held_slots[None, :]).reshape(
        experts * capacity, block_rows, TOP
    )
    send_map = jnp.any(matches, axis=2).astype(jnp.bfloat16)
    pieces, send_map = lax.optimization_barrier((pieces, send_map))
    summed = jnp.sum(pieces.astype(jnp.float32), axis=0)
    held_hidden = (held_residual.astype(jnp.float32) + summed).astype(jnp.bfloat16)
    outgoing = jnp.dot(send_map, held_hidden, preferred_element_type=jnp.float32).astype(jnp.bfloat16)
    hidden_in = lax.ppermute(held_hidden, everyone, perm=to_owner)
    arrived = lax.all_to_all(
        outgoing.reshape(experts, capacity, columns),
        everyone,
        split_axis=0,
        concat_axis=0,
        tiled=True,
    )
    arrived = arrived.reshape(groups, halves, groups, capacity, columns)
    gate = jnp.einsum(
        "gicsn,cnf->gisf", arrived, w_gate[0].reshape(groups, columns, -1),
        preferred_element_type=jnp.float32,
    ).reshape(members * capacity, -1)
    upper = jnp.einsum(
        "gicsn,cnf->gisf", arrived, w_up[0].reshape(groups, columns, -1),
        preferred_element_type=jnp.float32,
    ).reshape(members * capacity, -1)
    inner = (jax.nn.silu(gate) * upper).astype(jnp.bfloat16)
    results = jnp.einsum(
        "sf,fgc->gsc", inner, w_down[0].reshape(-1, groups, columns),
        preferred_element_type=jnp.float32,
    ).astype(jnp.bfloat16)
    returned = lax.all_to_all(
        results.reshape(experts, capacity, columns),
        everyone,
        split_axis=0,
        concat_axis=0,
        tiled=True,
    )
    returned = returned.reshape(experts * capacity, columns)
    slots = route(expert_ids).reshape(block_rows, TOP)
    gate_hi = route_gates.astype(jnp.bfloat16)
    gate_lo = (route_gates - gate_hi.astype(jnp.float32)).astype(jnp.bfloat16)
    hit = slots[:, :, None] == positions[None, None, :]
    zero = jnp.zeros((), jnp.bfloat16)
    map_hi = jnp.sum(jnp.where(hit, gate_hi[:, :, None], zero), axis=1)
    map_lo = jnp.sum(jnp.where(hit, gate_lo[:, :, None], zero), axis=1)
    mixed = jnp.dot(map_hi, returned, preferred_element_type=jnp.float32) + jnp.dot(
        map_lo, returned, preferred_element_type=jnp.float32
    )
    return (hidden_in.astype(jnp.float32) + mixed).astype(jnp.bfloat16)


def solution(mesh):
    in_specs = (
        P(("group", "member"), None, None),
        P(("group", "member"), None, None),
        P(("group", "member"), None),
        P(("group", "member")),
        P("member", None, None),
        P("member", "group"),
        P("member", "group"),
        P("member", None),
        P("member", None),
        P(("group", "member"), None, None),
        P(("group", "member"), None, None),
        P(("group", "member"), None, None),
    )
    out_specs = P("member", "group")
    return jax.shard_map(
        per_device, mesh=mesh, in_specs=in_specs, out_specs=out_specs, check_vma=False
    )
```

```python
import jax
import jax.numpy as jnp
from jax import lax
from jax.sharding import PartitionSpec as P

ROPE = 64
VHEAD = 128
TOP = 8
BEAM = 4


def per_device(
    queries,
    latent_cache,
    new_key,
    parent_beam,
    value_up,
    out_proj,
    residual,
    expert_ids,
    route_gates,
    w_gate,
    w_up,
    w_down,
):
    rows = queries.shape[0]
    latent = value_up.shape[1]
    members = lax.axis_size("member")
    groups = lax.axis_size("group")
    experts = groups * members
    columns = out_proj.shape[1]
    scale = (VHEAD + ROPE) ** (-0.5)
    context = latent_cache.shape[1]
    width = latent_cache.shape[2]
    beams = latent_cache.reshape(rows // BEAM, BEAM, context, width)
    chosen = parent_beam.reshape(rows // BEAM, BEAM, 1, 1)
    held = jnp.broadcast_to(beams[:, BEAM - 1 : BEAM], beams.shape)
    for beam in range(BEAM - 2, -1, -1):
        held = jnp.where(chosen == beam, beams[:, beam : beam + 1], held)
    held = held.reshape(rows, context, width)
    scores = jnp.einsum("rhw,rcw->rhc", queries, held, preferred_element_type=jnp.float32) * scale
    own = jnp.einsum("rhw,rw->rh", queries, new_key, preferred_element_type=jnp.float32) * scale
    top = jnp.maximum(jnp.max(scores, axis=-1), own)
    shifted = jnp.exp(scores - top[:, :, None])
    own_shifted = jnp.exp(own - top)
    total = jnp.sum(shifted, axis=-1) + own_shifted
    weights = (shifted / total[:, :, None]).astype(jnp.bfloat16)
    own_weight = (own_shifted / total).astype(jnp.bfloat16)
    mixed_cache = jnp.einsum(
        "rhc,rcl->rhl", weights, held[:, :, :latent], preferred_element_type=jnp.float32
    )
    mixed_new = own_weight.astype(jnp.float32)[:, :, None] * new_key[:, None, :latent].astype(jnp.float32)
    latent_out = (mixed_cache + mixed_new).astype(jnp.bfloat16)
    by_heads = lax.all_to_all(latent_out, "member", split_axis=1, concat_axis=0, tiled=True)
    per_head = jnp.einsum(
        "rhl,hlv->rhv", by_heads, value_up, preferred_element_type=jnp.float32
    ).astype(jnp.bfloat16)
    per_head = per_head.reshape(per_head.shape[0], per_head.shape[1] * per_head.shape[2])
    weights_all = lax.all_gather(out_proj, "group", axis=0, tiled=False)
    halves = per_head.shape[0] // residual.shape[0]
    pieces = jnp.einsum(
        "irk,ckn->icrn",
        per_head.reshape(halves, -1, per_head.shape[1]),
        weights_all,
        preferred_element_type=jnp.float32,
    ).astype(jnp.bfloat16).reshape(members, -1, columns)
    pieces = lax.all_to_all(pieces, "member", split_axis=0, concat_axis=0, tiled=True)
    block_rows = residual.shape[0]
    capacity = max(2, 2 * rows * TOP // members)
    positions = jnp.arange(experts * capacity, dtype=jnp.int32)
    to_owner = [
        (g * members + m, (m % groups) * members + (m // groups) + halves * g)
        for g in range(groups)
        for m in range(members)
    ]
    to_holder = [(b, a) for a, b in to_owner]
    everyone = ("group", "member")
    held_residual = lax.ppermute(residual, everyone, perm=to_holder)
    held_ids = lax.ppermute(expert_ids, everyone, perm=to_holder)

    def route(ids):
        flat_ids = ids.reshape(-1)
        onehot = (flat_ids[:, None] == jnp.arange(experts, dtype=jnp.int32)[None, :]).astype(jnp.int32)
        ranking = jnp.sum((jnp.cumsum(onehot, axis=0) - onehot) * onehot, axis=1)
        return flat_ids * capacity + ranking

    held_slots = route(held_ids)
    matches = (positions[:, None] == held_slots[None, :]).reshape(
        experts * capacity, block_rows, TOP
    )
    send_map = jnp.any(matches, axis=2).astype(jnp.bfloat16)
    pieces, send_map = lax.optimization_barrier((pieces, send_map))
    summed = jnp.sum(pieces.astype(jnp.float32), axis=0)
    held_hidden = (held_residual.astype(jnp.float32) + summed).astype(jnp.bfloat16)
    outgoing = jnp.dot(send_map, held_hidden, preferred_element_type=jnp.float32).astype(jnp.bfloat16)
    hidden_in = lax.ppermute(held_hidden, everyone, perm=to_owner)
    arrived = lax.all_to_all(
        outgoing.reshape(experts, capacity, columns),
        everyone,
        split_axis=0,
        concat_axis=0,
        tiled=True,
    )
    arrived = arrived.reshape(groups, halves, groups, capacity, columns)
    gate_w = w_gate[0].reshape(groups, columns, -1)
    up_w = w_up[0].reshape(groups, columns, -1)
    gate = None
    upper = None
    for c in range(groups):
        block = arrived[:, :, c].reshape(members * capacity, columns)
        g_part = jnp.dot(block, gate_w[c], preferred_element_type=jnp.float32)
        u_part = jnp.dot(block, up_w[c], preferred_element_type=jnp.float32)
        gate = g_part if gate is None else gate + g_part
        upper = u_part if upper is None else upper + u_part
    inner = (jax.nn.silu(gate) * upper).astype(jnp.bfloat16)
    results = jnp.einsum(
        "sf,fgc->gsc", inner, w_down[0].reshape(-1, groups, columns),
        preferred_element_type=jnp.float32,
    ).astype(jnp.bfloat16)
    returned = lax.all_to_all(
        results.reshape(experts, capacity, columns),
        everyone,
        split_axis=0,
        concat_axis=0,
        tiled=True,
    )
    returned = returned.reshape(experts * capacity, columns)
    slots = route(expert_ids).reshape(block_rows, TOP)
    gate_hi = route_gates.astype(jnp.bfloat16)
    gate_lo = (route_gates - gate_hi.astype(jnp.float32)).astype(jnp.bfloat16)
    hit = slots[:, :, None] == positions[None, None, :]
    zero = jnp.zeros((), jnp.bfloat16)
    map_hi = jnp.sum(jnp.where(hit, gate_hi[:, :, None], zero), axis=1)
    map_lo = jnp.sum(jnp.where(hit, gate_lo[:, :, None], zero), axis=1)
    mixed = jnp.dot(map_hi, returned, preferred_element_type=jnp.float32) + jnp.dot(
        map_lo, returned, preferred_element_type=jnp.float32
    )
    return (hidden_in.astype(jnp.float32) + mixed).astype(jnp.bfloat16)


def solution(mesh):
    in_specs = (
        P(("group", "member"), None, None),
        P(("group", "member"), None, None),
        P(("group", "member"), None),
        P(("group", "member")),
        P("member", None, None),
        P("member", "group"),
        P("member", "group"),
        P("member", None),
        P("member", None),
        P(("group", "member"), None, None),
        P(("group", "member"), None, None),
        P(("group", "member"), None, None),
    )
    out_specs = P("member", "group")
    return jax.shard_map(
        per_device, mesh=mesh, in_specs=in_specs, out_specs=out_specs, check_vma=False
    )
```

```python
import jax
import jax.numpy as jnp
from jax import lax
from jax.sharding import PartitionSpec as P

ROPE = 64
VHEAD = 128
TOP = 8
BEAM = 4


def per_device(
    queries,
    latent_cache,
    new_key,
    parent_beam,
    value_up,
    out_proj,
    residual,
    expert_ids,
    route_gates,
    w_gate,
    w_up,
    w_down,
):
    rows = queries.shape[0]
    latent = value_up.shape[1]
    members = lax.axis_size("member")
    groups = lax.axis_size("group")
    experts = groups * members
    columns = out_proj.shape[1]
    scale = (VHEAD + ROPE) ** (-0.5)
    context = latent_cache.shape[1]
    width = latent_cache.shape[2]
    beams = latent_cache.reshape(rows // BEAM, BEAM, context, width)
    chosen = parent_beam.reshape(rows // BEAM, BEAM, 1, 1)
    held = jnp.broadcast_to(beams[:, BEAM - 1 : BEAM], beams.shape)
    for beam in range(BEAM - 2, -1, -1):
        held = jnp.where(chosen == beam, beams[:, beam : beam + 1], held)
    held = held.reshape(rows, context, width)
    scores = jnp.einsum("rhw,rcw->rhc", queries, held, preferred_element_type=jnp.float32) * scale
    own = jnp.einsum("rhw,rw->rh", queries, new_key, preferred_element_type=jnp.float32) * scale
    top = jnp.maximum(jnp.max(scores, axis=-1), own)
    shifted = jnp.exp(scores - top[:, :, None])
    own_shifted = jnp.exp(own - top)
    total = jnp.sum(shifted, axis=-1) + own_shifted
    weights = (shifted / total[:, :, None]).astype(jnp.bfloat16)
    own_weight = (own_shifted / total).astype(jnp.bfloat16)
    mixed_cache = jnp.einsum(
        "rhc,rcl->rhl", weights, held[:, :, :latent], preferred_element_type=jnp.float32
    )
    mixed_new = own_weight.astype(jnp.float32)[:, :, None] * new_key[:, None, :latent].astype(jnp.float32)
    latent_out = (mixed_cache + mixed_new).astype(jnp.bfloat16)
    by_heads = lax.all_to_all(latent_out, "member", split_axis=1, concat_axis=0, tiled=True)
    per_head = jnp.einsum(
        "rhl,hlv->rhv", by_heads, value_up, preferred_element_type=jnp.float32
    ).astype(jnp.bfloat16)
    per_head = per_head.reshape(per_head.shape[0], per_head.shape[1] * per_head.shape[2])
    weights_all = lax.all_gather(out_proj, "group", axis=0, tiled=False)
    halves = per_head.shape[0] // residual.shape[0]
    pieces = jnp.einsum(
        "irk,ckn->icrn",
        per_head.reshape(halves, -1, per_head.shape[1]),
        weights_all,
        preferred_element_type=jnp.float32,
    ).astype(jnp.bfloat16).reshape(members, -1, columns)
    pieces = lax.all_to_all(pieces, "member", split_axis=0, concat_axis=0, tiled=True)
    block_rows = residual.shape[0]
    capacity = max(2, 2 * rows * TOP // members)
    positions = jnp.arange(experts * capacity, dtype=jnp.int32)
    to_owner = [
        (g * members + m, (m % groups) * members + (m // groups) + halves * g)
        for g in range(groups)
        for m in range(members)
    ]
    to_holder = [(b, a) for a, b in to_owner]
    everyone = ("group", "member")
    held_residual = lax.ppermute(residual, everyone, perm=to_holder)
    held_ids = lax.ppermute(expert_ids, everyone, perm=to_holder)

    def route(ids):
        flat_ids = ids.reshape(-1)
        onehot = (flat_ids[:, None] == jnp.arange(experts, dtype=jnp.int32)[None, :]).astype(jnp.int32)
        ranking = jnp.sum((jnp.cumsum(onehot, axis=0) - onehot) * onehot, axis=1)
        return flat_ids * capacity + ranking

    held_slots = route(held_ids)
    matches = (positions[:, None] == held_slots[None, :]).reshape(
        experts * capacity, block_rows, TOP
    )
    send_map = jnp.any(matches, axis=2).astype(jnp.bfloat16)
    pieces, send_map = lax.optimization_barrier((pieces, send_map))
    summed = jnp.sum(pieces.astype(jnp.float32), axis=0)
    held_hidden = (held_residual.astype(jnp.float32) + summed).astype(jnp.bfloat16)
    outgoing = jnp.dot(send_map, held_hidden, preferred_element_type=jnp.float32).astype(jnp.bfloat16)
    hidden_in = lax.ppermute(held_hidden, everyone, perm=to_owner)
    arrived = lax.all_to_all(
        outgoing.reshape(experts, capacity, columns),
        everyone,
        split_axis=0,
        concat_axis=0,
        tiled=True,
    )
    arrived = arrived.reshape(groups, halves, groups, capacity, columns)
    arrived = arrived.transpose(2, 0, 1, 3, 4).reshape(groups, members * capacity, columns)
    gate = jnp.einsum(
        "csn,cnf->sf", arrived, w_gate[0].reshape(groups, columns, -1),
        preferred_element_type=jnp.float32,
    )
    upper = jnp.einsum(
        "csn,cnf->sf", arrived, w_up[0].reshape(groups, columns, -1),
        preferred_element_type=jnp.float32,
    )
    inner = (jax.nn.silu(gate) * upper).astype(jnp.bfloat16)
    results = jnp.einsum(
        "sf,fgc->gsc", inner, w_down[0].reshape(-1, groups, columns),
        preferred_element_type=jnp.float32,
    ).astype(jnp.bfloat16)
    returned = lax.all_to_all(
        results.reshape(experts, capacity, columns),
        everyone,
        split_axis=0,
        concat_axis=0,
        tiled=True,
    )
    returned = returned.reshape(experts * capacity, columns)
    slots = route(expert_ids).reshape(block_rows, TOP)
    gate_hi = route_gates.astype(jnp.bfloat16)
    gate_lo = (route_gates - gate_hi.astype(jnp.float32)).astype(jnp.bfloat16)
    hit = slots[:, :, None] == positions[None, None, :]
    zero = jnp.zeros((), jnp.bfloat16)
    map_hi = jnp.sum(jnp.where(hit, gate_hi[:, :, None], zero), axis=1)
    map_lo = jnp.sum(jnp.where(hit, gate_lo[:, :, None], zero), axis=1)
    mixed = jnp.dot(map_hi, returned, preferred_element_type=jnp.float32) + jnp.dot(
        map_lo, returned, preferred_element_type=jnp.float32
    )
    return (hidden_in.astype(jnp.float32) + mixed).astype(jnp.bfloat16)


def solution(mesh):
    in_specs = (
        P(("group", "member"), None, None),
        P(("group", "member"), None, None),
        P(("group", "member"), None),
        P(("group", "member")),
        P("member", None, None),
        P("member", "group"),
        P("member", "group"),
        P("member", None),
        P("member", None),
        P(("group", "member"), None, None),
        P(("group", "member"), None, None),
        P(("group", "member"), None, None),
    )
    out_specs = P("member", "group")
    return jax.shard_map(
        per_device, mesh=mesh, in_specs=in_specs, out_specs=out_specs, check_vma=False
    )
```

```python
import jax
import jax.numpy as jnp
from jax import lax
from jax.sharding import PartitionSpec as P

ROPE = 64
VHEAD = 128
TOP = 8
BEAM = 4


def per_device(
    queries,
    latent_cache,
    new_key,
    parent_beam,
    value_up,
    out_proj,
    residual,
    expert_ids,
    route_gates,
    w_gate,
    w_up,
    w_down,
):
    rows = queries.shape[0]
    latent = value_up.shape[1]
    members = lax.axis_size("member")
    groups = lax.axis_size("group")
    experts = groups * members
    columns = out_proj.shape[1]
    scale = (VHEAD + ROPE) ** (-0.5)
    to_owner = [
        (g * members + m, (m % groups) * members + (m // groups) + (rows * members // residual.shape[0]) * g)
        for g in range(groups)
        for m in range(members)
    ]
    to_holder = [(b, a) for a, b in to_owner]
    everyone = ("group", "member")
    held_residual = lax.ppermute(residual, everyone, perm=to_holder)
    held_ids = lax.ppermute(expert_ids, everyone, perm=to_holder)

    context = latent_cache.shape[1]
    width = latent_cache.shape[2]
    beams = latent_cache.reshape(rows // BEAM, BEAM, context, width)
    chosen = parent_beam.reshape(rows // BEAM, BEAM, 1, 1)
    held = jnp.broadcast_to(beams[:, BEAM - 1 : BEAM], beams.shape)
    for beam in range(BEAM - 2, -1, -1):
        held = jnp.where(chosen == beam, beams[:, beam : beam + 1], held)
    held = held.reshape(rows, context, width)
    scores = jnp.einsum("rhw,rcw->rhc", queries, held, preferred_element_type=jnp.float32) * scale
    own = jnp.einsum("rhw,rw->rh", queries, new_key, preferred_element_type=jnp.float32) * scale
    top = jnp.maximum(jnp.max(scores, axis=-1), own)
    shifted = jnp.exp(scores - top[:, :, None])
    own_shifted = jnp.exp(own - top)
    total = jnp.sum(shifted, axis=-1) + own_shifted
    weights = (shifted / total[:, :, None]).astype(jnp.bfloat16)
    own_weight = (own_shifted / total).astype(jnp.bfloat16)
    mixed_cache = jnp.einsum(
        "rhc,rcl->rhl", weights, held[:, :, :latent], preferred_element_type=jnp.float32
    )
    mixed_new = own_weight.astype(jnp.float32)[:, :, None] * new_key[:, None, :latent].astype(jnp.float32)
    latent_out = (mixed_cache + mixed_new).astype(jnp.bfloat16)
    by_heads = lax.all_to_all(latent_out, "member", split_axis=1, concat_axis=0, tiled=True)
    by_heads, held_ids, held_residual = lax.optimization_barrier((by_heads, held_ids, held_residual))
    per_head = jnp.einsum(
        "rhl,hlv->rhv", by_heads, value_up, preferred_element_type=jnp.float32
    ).astype(jnp.bfloat16)
    per_head = per_head.reshape(per_head.shape[0], per_head.shape[1] * per_head.shape[2])
    weights_all = lax.all_gather(out_proj, "group", axis=0, tiled=False)
    halves = per_head.shape[0] // residual.shape[0]
    pieces = jnp.einsum(
        "irk,ckn->icrn",
        per_head.reshape(halves, -1, per_head.shape[1]),
        weights_all,
        preferred_element_type=jnp.float32,
    ).astype(jnp.bfloat16).reshape(members, -1, columns)
    pieces = lax.all_to_all(pieces, "member", split_axis=0, concat_axis=0, tiled=True)
    block_rows = residual.shape[0]
    capacity = max(2, 2 * rows * TOP // members)
    positions = jnp.arange(experts * capacity, dtype=jnp.int32)
    def route(ids):
        flat_ids = ids.reshape(-1)
        onehot = (flat_ids[:, None] == jnp.arange(experts, dtype=jnp.int32)[None, :]).astype(jnp.int32)
        ranking = jnp.sum((jnp.cumsum(onehot, axis=0) - onehot) * onehot, axis=1)
        return flat_ids * capacity + ranking

    held_slots = route(held_ids)
    matches = (positions[:, None] == held_slots[None, :]).reshape(
        experts * capacity, block_rows, TOP
    )
    send_map = jnp.any(matches, axis=2).astype(jnp.bfloat16)
    pieces, send_map = lax.optimization_barrier((pieces, send_map))
    summed = jnp.sum(pieces.astype(jnp.float32), axis=0)
    held_hidden = (held_residual.astype(jnp.float32) + summed).astype(jnp.bfloat16)
    outgoing = jnp.dot(send_map, held_hidden, preferred_element_type=jnp.float32).astype(jnp.bfloat16)
    hidden_in = lax.ppermute(held_hidden, everyone, perm=to_owner)
    arrived = lax.all_to_all(
        outgoing.reshape(experts, capacity, columns),
        everyone,
        split_axis=0,
        concat_axis=0,
        tiled=True,
    )
    arrived = arrived.reshape(groups, halves, groups, capacity, columns)
    arrived = arrived.transpose(2, 0, 1, 3, 4).reshape(groups, members * capacity, columns)
    gate = jnp.einsum(
        "csn,cnf->sf", arrived, w_gate[0].reshape(groups, columns, -1),
        preferred_element_type=jnp.float32,
    )
    upper = jnp.einsum(
        "csn,cnf->sf", arrived, w_up[0].reshape(groups, columns, -1),
        preferred_element_type=jnp.float32,
    )
    inner = (jax.nn.silu(gate) * upper).astype(jnp.bfloat16)
    results = jnp.einsum(
        "sf,fgc->gsc", inner, w_down[0].reshape(-1, groups, columns),
        preferred_element_type=jnp.float32,
    ).astype(jnp.bfloat16)
    returned = lax.all_to_all(
        results.reshape(experts, capacity, columns),
        everyone,
        split_axis=0,
        concat_axis=0,
        tiled=True,
    )
    returned = returned.reshape(experts * capacity, columns)
    slots = route(expert_ids).reshape(block_rows, TOP)
    gate_hi = route_gates.astype(jnp.bfloat16)
    gate_lo = (route_gates - gate_hi.astype(jnp.float32)).astype(jnp.bfloat16)
    hit = slots[:, :, None] == positions[None, None, :]
    zero = jnp.zeros((), jnp.bfloat16)
    map_hi = jnp.sum(jnp.where(hit, gate_hi[:, :, None], zero), axis=1)
    map_lo = jnp.sum(jnp.where(hit, gate_lo[:, :, None], zero), axis=1)
    mixed = jnp.dot(map_hi, returned, preferred_element_type=jnp.float32) + jnp.dot(
        map_lo, returned, preferred_element_type=jnp.float32
    )
    return (hidden_in.astype(jnp.float32) + mixed).astype(jnp.bfloat16)


def solution(mesh):
    in_specs = (
        P(("group", "member"), None, None),
        P(("group", "member"), None, None),
        P(("group", "member"), None),
        P(("group", "member")),
        P("member", None, None),
        P("member", "group"),
        P("member", "group"),
        P("member", None),
        P("member", None),
        P(("group", "member"), None, None),
        P(("group", "member"), None, None),
        P(("group", "member"), None, None),
    )
    out_specs = P("member", "group")
    return jax.shard_map(
        per_device, mesh=mesh, in_specs=in_specs, out_specs=out_specs, check_vma=False
    )
```
